1024 devices in a mesh: sector: 32 (over y, z_hi, core), op: 32 (over z_lo, x).
Axes of the slice: x: 4, y: 4, z: 32 (z_hi: 4, z_lo: 8; z = z_hi * 8 + z_lo), core: 2. Of those that a mesh axis runs over, the one named last changes fastest.
Arguments:
- psi: bfloat16 [32, 512, 512], P('sector', 'op'), may hold values from -6 to 6
- in_sector: int32 [32, 32], P('sector'), may hold values from 0 to 31
- term_count: int32 [32, 32], P('sector', 'op'), may hold values from 1 to 4, as said below
- coef_index: int32 [32, 128], P('sector', 'op'), may hold values from 0 to 63
- left_index: int32 [32, 128], P('sector', 'op'), may hold values from 0 to 1
- term_values: float32 [64], replicated, may hold values from -0.9 to 0.9
- left_ops: bfloat16 [32, 2, 512, 512], P('sector'), may hold values from -0.25 to 0.25
- right_ops: bfloat16 [32, 128, 512, 512], P('sector', 'op'), may hold values from -0.25 to 0.25
Outputs:
- hpsi: float32 [32, 512, 512], P('sector', 'op')
The draws below stay inside these ranges and needn't reach their ends.
Inputs may be any that keep to these rules, and one draw needn't show every extreme that they name: `term_count`: some device has all 4 slots live in every draw.
All inputs are finite; a program needn't handle non-finite values.
Results may differ from the reference program's by a relative error of at most 0.0029.
Values may be sent and summed in bfloat16 or wider, within the bound.
No kernel may reach another device: no remote copies, remote signals or barrier semaphores. Data moves between devices by JAX's collectives and lax.ppermute only.
A program may use at most 32 MiB of HBM per device.

```python
import jax
import jax.numpy as jnp
from jax import lax

M = 512
TERMS = 4
NL = 2
NCOEF = 64
NS = 32
N_OP = 32


def draw_term_count(key, part):
    first, second = jax.random.split(key)
    level = jax.random.randint(first, (NS * N_OP,), 0, 8)
    counts = jnp.where(level == 0, TERMS, jnp.where(level < 3, min(2, TERMS), 1)).astype(jnp.int32)
    spot = jax.random.randint(second, (), 0, NS * N_OP)
    counts = counts.at[spot].set(TERMS)
    return counts.reshape(NS, N_OP)


def touch_ends(drawn, key, least, top_value):
    longest = drawn.shape.index(max(drawn.shape))
    spots = []
    for shift in (0, 1):
        where = [jax.random.randint(jax.random.fold_in(key, axis), (), 0, length) for axis, length in enumerate(drawn.shape)]
        where[longest] = (where[longest] + shift) % drawn.shape[longest]
        spots.append(tuple(where))
    return drawn.at[spots[0]].set(least).at[spots[1]].set(top_value)


def shard_levels(own_key, extent, cuts, low, largest):
    loudness, own = 1.0, jax.random.fold_in(own_key, 6)
    for position, parts in cuts:
        draws = jnp.exp(jax.random.uniform(jax.random.fold_in(own, position), (parts,), jnp.float32, low / len(cuts), largest / len(cuts)))
        loudness = loudness * jnp.repeat(draws, extent[position] // parts).reshape([-1 if axis == position else 1 for axis in range(len(extent))])
    return loudness


def scatter_about(stream_key, dims, width, bound, shards=(), held_as=jnp.bfloat16):
    factor_of = shard_levels(stream_key, dims, shards, -0.22, 0.18) if shards else 1.0
    values = jax.random.normal(stream_key, dims, jnp.float32) * width * factor_of
    return jnp.minimum(jnp.maximum(values, -bound), bound).astype(held_as)


def setup_inputs(seed: int = 0) -> dict:
    streams_of = jax.random.split(jax.random.key(seed), 9)
    return {
        "psi": scatter_about(streams_of[0], (NS, M, M), 1.0, 6.0, ((0, 32), (1, 32))),
        "in_sector": touch_ends(jax.random.randint(streams_of[1], (NS, N_OP), 0, NS), jax.random.fold_in(streams_of[1], 1), 0, NS - 1).astype(jnp.int32),
        "term_count": draw_term_count(jax.random.fold_in(streams_of[8], 71), 0),
        "coef_index": touch_ends(jax.random.randint(streams_of[3], (NS, N_OP * TERMS), 0, NCOEF), jax.random.fold_in(streams_of[3], 1), 0, NCOEF - 1).astype(jnp.int32),
        "left_index": touch_ends(jax.random.randint(streams_of[4], (NS, N_OP * TERMS), 0, NL), jax.random.fold_in(streams_of[4], 1), 0, NL - 1).astype(jnp.int32),
        "term_values": scatter_about(streams_of[5], (NCOEF,), 0.15, 0.9, (), jnp.float32),
        "left_ops": scatter_about(streams_of[6], (NS, NL, M, M), M ** -0.5, 0.25, ((0, 32),)),
        "right_ops": scatter_about(streams_of[7], (NS, N_OP * TERMS, M, M), M ** -0.5, 0.25, ((0, 32), (1, 32))),
    }


def reference(psi, in_sector, term_count, coef_index, left_index, term_values, left_ops, right_ops):
    def one_sector(sector):
        def add_term(total, slot):
            owner = slot // TERMS
            within = slot % TERMS
            live = within < term_count[sector, owner]

            def apply(carry):
                block = psi[in_sector[sector, owner]]
                half = jnp.dot(block, right_ops[sector, slot], preferred_element_type=jnp.float32).astype(jnp.bfloat16)
                left = left_ops[sector, left_index[sector, slot]]
                weight = term_values[coef_index[sector, slot]]
                return carry + weight * jnp.dot(left, half, preferred_element_type=jnp.float32)

            return lax.cond(live, apply, lambda carry: carry, total), None

        start = jnp.zeros((M, M), jnp.float32)
        total, unused = lax.scan(add_term, start, jnp.arange(N_OP * TERMS, dtype=jnp.int32))
        return total

    return lax.map(one_sector, jnp.arange(NS, dtype=jnp.int32))
```

```python
import jax
import jax.numpy as jnp
import numpy as np
from jax import lax
from jax.sharding import Mesh, PartitionSpec as P

GATHER = "h_czy"
REDUCE = "h_a2a"

SEC = ("y", "zh", "c")
OPX = ("zl", "x")


def gather_psi(psi):
    if GATHER == "ag":
        g = lax.all_gather(psi, SEC, axis=0, tiled=True)
        return g, lambda s: s
    if GATHER == "h_cyz":
        g = lax.all_gather(psi, "c", axis=0, tiled=True)
        g = lax.all_gather(g, "y", axis=0, tiled=True)
        g = lax.all_gather(g, "zh", axis=0, tiled=True)
        return g, lambda s: (s % 8) // 2 * 8 + s // 8 * 2 + s % 2
    if GATHER == "h_czy":
        g = lax.all_gather(psi, "c", axis=0, tiled=True)
        g = lax.all_gather(g, "zh", axis=0, tiled=True)
        g = lax.all_gather(g, "y", axis=0, tiled=True)
        return g, lambda s: s
    if GATHER == "a2a":
        n = 32
        rep = jnp.broadcast_to(psi, (n,) + psi.shape[1:])
        g = lax.all_to_all(rep, SEC, split_axis=0, concat_axis=0, tiled=True)
        return g, lambda s: s
    raise ValueError


def reduce_out(total, slab_rows, width):
    if REDUCE == "rs":
        return lax.psum_scatter(total, OPX, scatter_dimension=0, tiled=True)
    if REDUCE == "a2a":
        parts = lax.all_to_all(total.reshape(32, slab_rows, width), OPX, split_axis=0, concat_axis=0, tiled=True)
        return jnp.sum(parts, axis=0)
    if REDUCE == "h_rs":
        t = total.reshape(8, 4, slab_rows, width).transpose(1, 0, 2, 3)
        t = lax.psum_scatter(t, "x", scatter_dimension=0, tiled=True)
        t = lax.psum_scatter(t.reshape(8, slab_rows, width), "zl", scatter_dimension=0, tiled=True)
        return t
    if REDUCE == "h_a2a":
        t = total.reshape(8, 4, slab_rows, width).transpose(1, 0, 2, 3)
        t = lax.all_to_all(t, "x", split_axis=0, concat_axis=0, tiled=True)
        t = jnp.sum(t, axis=0)
        t = lax.all_to_all(t, "zl", split_axis=0, concat_axis=0, tiled=True)
        return jnp.sum(t, axis=0)
    if REDUCE == "h_rs_a2a":
        t = total.reshape(8, 4, slab_rows, width).transpose(1, 0, 2, 3)
        t = lax.psum_scatter(t, "x", scatter_dimension=0, tiled=True).reshape(8, slab_rows, width)
        t = lax.all_to_all(t, "zl", split_axis=0, concat_axis=0, tiled=True)
        return jnp.sum(t, axis=0)
    if REDUCE == "h_a2a_rs":
        t = total.reshape(8, 4, slab_rows, width).transpose(1, 0, 2, 3)
        t = lax.all_to_all(t, "x", split_axis=0, concat_axis=0, tiled=True)
        t = jnp.sum(t, axis=0)
        return lax.psum_scatter(t, "zl", scatter_dimension=0, tiled=True)
    raise ValueError


def body(psi, in_sector, term_count, coef_index, left_index, term_values, left_ops, right_ops):
    ops = 32
    slab_rows = psi.shape[1]
    width = psi.shape[2]
    slabs, remap = gather_psi(psi)
    wanted = remap(in_sector[0])
    outgoing = jnp.take(slabs, wanted, axis=0)
    arrived = lax.all_to_all(outgoing, OPX, split_axis=0, concat_axis=0, tiled=True)
    block = arrived.reshape(ops * slab_rows, width)
    slots = right_ops.shape[1]
    count = term_count[0, 0]
    table_size = term_values.shape[0]
    onehot = (coef_index[0][:, None] == jnp.arange(table_size, dtype=jnp.int32)[None, :]).astype(jnp.float32)
    weights = jnp.sum(onehot * term_values[None, :], axis=1)
    live = jnp.arange(slots, dtype=jnp.int32) < count
    weights = jnp.where(live, weights, 0.0)
    lefts = [lax.dynamic_index_in_dim(left_ops[0], left_index[0, k], 0, keepdims=False) for k in range(slots)]
    halves = [jnp.dot(block, right_ops[0, k], preferred_element_type=jnp.float32).astype(jnp.bfloat16) for k in range(slots)]
    total = jnp.zeros((ops * slab_rows, width), jnp.float32)
    for k in range(slots):
        total = total + weights[k] * jnp.dot(lefts[k], halves[k], preferred_element_type=jnp.float32)
    mine = reduce_out(total, slab_rows, width)
    return mine.reshape(1, slab_rows, width)


def solution(mesh):
    devs = np.asarray(mesh.devices).reshape(4, 4, 2, 8, 4)
    fine = Mesh(devs, ("y", "zh", "c", "zl", "x"))
    in_specs = (
        P(SEC, OPX, None),
        P(SEC, None),
        P(SEC, OPX),
        P(SEC, OPX),
        P(SEC, OPX),
        P(),
        P(SEC, None, None, None),
        P(SEC, OPX, None, None),
    )
    out_specs = P(SEC, OPX, None)
    return jax.shard_map(body, mesh=fine, in_specs=in_specs, out_specs=out_specs, check_vma=False)
```

```python
import jax
import jax.numpy as jnp
import numpy as np
from jax import lax
from jax.sharding import Mesh, PartitionSpec as P

GATHER = "h_czy"
REDUCE = "h_a2a_xbf"
ROUTE = "flat"
COMPUTE = "batch"

SEC = ("y", "zh", "c")
OPX = ("zl", "x")


def gather_psi(psi):
    if GATHER == "ag":
        g = lax.all_gather(psi, SEC, axis=0, tiled=True)
        return g, lambda s: s
    if GATHER == "h_cyz":
        g = lax.all_gather(psi, "c", axis=0, tiled=True)
        g = lax.all_gather(g, "y", axis=0, tiled=True)
        g = lax.all_gather(g, "zh", axis=0, tiled=True)
        return g, lambda s: (s % 8) // 2 * 8 + s // 8 * 2 + s % 2
    if GATHER == "h_czy":
        g = lax.all_gather(psi, "c", axis=0, tiled=True)
        g = lax.all_gather(g, "zh", axis=0, tiled=True)
        g = lax.all_gather(g, "y", axis=0, tiled=True)
        return g, lambda s: s
    if GATHER == "h_zyc":
        g = lax.all_gather(psi, "zh", axis=0, tiled=True)
        g = lax.all_gather(g, "y", axis=0, tiled=True)
        g = lax.all_gather(g, "c", axis=0, tiled=True)
        return g, lambda s: (s % 2) * 16 + (s // 8) * 4 + (s % 8) // 2
    if GATHER == "h_yzc":
        g = lax.all_gather(psi, "y", axis=0, tiled=True)
        g = lax.all_gather(g, "zh", axis=0, tiled=True)
        g = lax.all_gather(g, "c", axis=0, tiled=True)
        return g, lambda s: (s % 2) * 16 + ((s % 8) // 2) * 4 + s // 8
    if GATHER == "c_yz":
        g = lax.all_gather(psi, "c", axis=0, tiled=True)
        g = lax.all_gather(g, ("y", "zh"), axis=0, tiled=True)
        return g, lambda s: s
    if GATHER == "c_zpsum_y":
        g = lax.all_gather(psi, "c", axis=0, tiled=True)
        zi = lax.axis_index("zh")
        buf = jnp.zeros((4,) + g.shape, g.dtype)
        buf = lax.dynamic_update_index_in_dim(buf, g, zi, 0)
        g = lax.psum(buf, "zh").reshape((8,) + g.shape[1:])
        g = lax.all_gather(g, "y", axis=0, tiled=True)
        return g, lambda s: s
    if GATHER == "c_za2a_y":
        g = lax.all_gather(psi, "c", axis=0, tiled=True)
        rep = jnp.broadcast_to(g[None], (4,) + g.shape).reshape((8,) + g.shape[1:])
        g = lax.all_to_all(rep, "zh", split_axis=0, concat_axis=0, tiled=True)
        g = lax.all_gather(g, "y", axis=0, tiled=True)
        return g, lambda s: s
    if GATHER == "a2a":
        n = 32
        rep = jnp.broadcast_to(psi, (n,) + psi.shape[1:])
        g = lax.all_to_all(rep, SEC, split_axis=0, concat_axis=0, tiled=True)
        return g, lambda s: s
    raise ValueError


def reduce_out(total, slab_rows, width):
    if REDUCE == "rs":
        return lax.psum_scatter(total, OPX, scatter_dimension=0, tiled=True)
    if REDUCE == "a2a":
        parts = lax.all_to_all(total.reshape(32, slab_rows, width), OPX, split_axis=0, concat_axis=0, tiled=True)
        return jnp.sum(parts, axis=0)
    if REDUCE == "h_rs":
        t = total.reshape(8, 4, slab_rows, width).transpose(1, 0, 2, 3)
        t = lax.psum_scatter(t, "x", scatter_dimension=0, tiled=True)
        t = lax.psum_scatter(t.reshape(8, slab_rows, width), "zl", scatter_dimension=0, tiled=True)
        return t
    if REDUCE == "h_a2a_zbf":
        t = total.reshape(8, 4, slab_rows, width).transpose(1, 0, 2, 3)
        t = lax.all_to_all(t, "x", split_axis=0, concat_axis=0, tiled=True)
        t = jnp.sum(t, axis=0).astype(jnp.bfloat16)
        t = lax.all_to_all(t, "zl", split_axis=0, concat_axis=0, tiled=True)
        return jnp.sum(t.astype(jnp.float32), axis=0)
    if REDUCE == "h_a2a_xbf":
        t = total.reshape(8, 4, slab_rows, width).transpose(1, 0, 2, 3).astype(jnp.bfloat16)
        t = lax.all_to_all(t, "x", split_axis=0, concat_axis=0, tiled=True)
        t = jnp.sum(t.astype(jnp.float32), axis=0)
        t = lax.all_to_all(t, "zl", split_axis=0, concat_axis=0, tiled=True)
        return jnp.sum(t, axis=0)
    if REDUCE == "h_a2a":
        t = total.reshape(8, 4, slab_rows, width).transpose(1, 0, 2, 3)
        t = lax.all_to_all(t, "x", split_axis=0, concat_axis=0, tiled=True)
        t = jnp.sum(t, axis=0)
        t = lax.all_to_all(t, "zl", split_axis=0, concat_axis=0, tiled=True)
        return jnp.sum(t, axis=0)
    if REDUCE == "h_rs_a2a":
        t = total.reshape(8, 4, slab_rows, width).transpose(1, 0, 2, 3)
        t = lax.psum_scatter(t, "x", scatter_dimension=0, tiled=True).reshape(8, slab_rows, width)
        t = lax.all_to_all(t, "zl", split_axis=0, concat_axis=0, tiled=True)
        return jnp.sum(t, axis=0)
    if REDUCE == "h_a2a_rs":
        t = total.reshape(8, 4, slab_rows, width).transpose(1, 0, 2, 3)
        t = lax.all_to_all(t, "x", split_axis=0, concat_axis=0, tiled=True)
        t = jnp.sum(t, axis=0)
        return lax.psum_scatter(t, "zl", scatter_dimension=0, tiled=True)
    raise ValueError


def body(psi, in_sector, term_count, coef_index, left_index, term_values, left_ops, right_ops):
    ops = 32
    slab_rows = psi.shape[1]
    width = psi.shape[2]
    slabs, remap = gather_psi(psi)
    wanted = remap(in_sector[0])
    outgoing = jnp.take(slabs, wanted, axis=0)
    if ROUTE == "flat":
        arrived = lax.all_to_all(outgoing, OPX, split_axis=0, concat_axis=0, tiled=True)
    else:
        t = outgoing.reshape(8, 4, slab_rows, width).transpose(1, 0, 2, 3)
        t = lax.all_to_all(t, "x", split_axis=0, concat_axis=0, tiled=True)
        t = t.transpose(1, 0, 2, 3)
        t = lax.all_to_all(t, "zl", split_axis=0, concat_axis=0, tiled=True)
        arrived = t.reshape(32, slab_rows, width)
    block = arrived.reshape(ops * slab_rows, width)
    slots = right_ops.shape[1]
    count = term_count[0, 0]
    table_size = term_values.shape[0]
    onehot = (coef_index[0][:, None] == jnp.arange(table_size, dtype=jnp.int32)[None, :]).astype(jnp.float32)
    weights = jnp.sum(onehot * term_values[None, :], axis=1)
    live = jnp.arange(slots, dtype=jnp.int32) < count
    weights = jnp.where(live, weights, 0.0)
    if COMPUTE == "loop":
        lefts = [lax.dynamic_index_in_dim(left_ops[0], left_index[0, k], 0, keepdims=False) for k in range(slots)]
        halves = [jnp.dot(block, right_ops[0, k], preferred_element_type=jnp.float32).astype(jnp.bfloat16) for k in range(slots)]
        total = jnp.zeros((ops * slab_rows, width), jnp.float32)
        for k in range(slots):
            total = total + weights[k] * jnp.dot(lefts[k], halves[k], preferred_element_type=jnp.float32)
    else:
        lefts = jnp.take(left_ops[0], left_index[0], axis=0)
        halves = jnp.einsum("ij,kjl->kil", block, right_ops[0], preferred_element_type=jnp.float32).astype(jnp.bfloat16)
        prods = jnp.einsum("kij,kjl->kil", lefts, halves, preferred_element_type=jnp.float32)
        total = jnp.sum(weights[:, None, None] * prods, axis=0)
    mine = reduce_out(total, slab_rows, width)
    return mine.reshape(1, slab_rows, width)


def solution(mesh):
    devs = np.asarray(mesh.devices).reshape(4, 4, 2, 8, 4)
    fine = Mesh(devs, ("y", "zh", "c", "zl", "x"))
    in_specs = (
        P(SEC, OPX, None),
        P(SEC, None),
        P(SEC, OPX),
        P(SEC, OPX),
        P(SEC, OPX),
        P(),
        P(SEC, None, None, None),
        P(SEC, OPX, None, None),
    )
    out_specs = P(SEC, OPX, None)
    return jax.shard_map(body, mesh=fine, in_specs=in_specs, out_specs=out_specs, check_vma=False)
```

```python
import jax
import jax.numpy as jnp
import numpy as np
from jax import lax
from jax.sharding import Mesh, PartitionSpec as P

GATHER = "h_czy"
REDUCE = "h_a2a_xbf"
ROUTE = "flat"
COMPUTE = "batch"
TAKE = "clip"

SEC = ("y", "zh", "c")
OPX = ("zl", "x")


def gather_psi(psi):
    if GATHER == "ag":
        g = lax.all_gather(psi, SEC, axis=0, tiled=True)
        return g, lambda s: s
    if GATHER == "h_cyz":
        g = lax.all_gather(psi, "c", axis=0, tiled=True)
        g = lax.all_gather(g, "y", axis=0, tiled=True)
        g = lax.all_gather(g, "zh", axis=0, tiled=True)
        return g, lambda s: (s % 8) // 2 * 8 + s // 8 * 2 + s % 2
    if GATHER == "h_czy":
        g = lax.all_gather(psi, "c", axis=0, tiled=True)
        g = lax.all_gather(g, "zh", axis=0, tiled=True)
        g = lax.all_gather(g, "y", axis=0, tiled=True)
        return g, lambda s: s
    if GATHER == "h_zyc":
        g = lax.all_gather(psi, "zh", axis=0, tiled=True)
        g = lax.all_gather(g, "y", axis=0, tiled=True)
        g = lax.all_gather(g, "c", axis=0, tiled=True)
        return g, lambda s: (s % 2) * 16 + (s // 8) * 4 + (s % 8) // 2
    if GATHER == "h_yzc":
        g = lax.all_gather(psi, "y", axis=0, tiled=True)
        g = lax.all_gather(g, "zh", axis=0, tiled=True)
        g = lax.all_gather(g, "c", axis=0, tiled=True)
        return g, lambda s: (s % 2) * 16 + ((s % 8) // 2) * 4 + s // 8
    if GATHER == "c_zpp_y":
        g = lax.all_gather(psi, "c", axis=0, tiled=True)
        zi = lax.axis_index("zh")
        recv = [g] + [lax.ppermute(g, "zh", [(i, (i + d) % 4) for i in range(4)]) for d in range(1, 4)]
        st = jnp.stack(recv)
        order = (zi - jnp.arange(4)) % 4
        g = jnp.take(st, order, axis=0, mode="clip").reshape((8,) + g.shape[1:])
        g = lax.all_gather(g, "y", axis=0, tiled=True)
        return g, lambda s: s
    if GATHER == "c_yz":
        g = lax.all_gather(psi, "c", axis=0, tiled=True)
        g = lax.all_gather(g, ("y", "zh"), axis=0, tiled=True)
        return g, lambda s: s
    if GATHER == "c_zpsum_y":
        g = lax.all_gather(psi, "c", axis=0, tiled=True)
        zi = lax.axis_index("zh")
        buf = jnp.zeros((4,) + g.shape, g.dtype)
        buf = lax.dynamic_update_index_in_dim(buf, g, zi, 0)
        g = lax.psum(buf, "zh").reshape((8,) + g.shape[1:])
        g = lax.all_gather(g, "y", axis=0, tiled=True)
        return g, lambda s: s
    if GATHER == "c_za2a_y":
        g = lax.all_gather(psi, "c", axis=0, tiled=True)
        rep = jnp.broadcast_to(g[None], (4,) + g.shape).reshape((8,) + g.shape[1:])
        g = lax.all_to_all(rep, "zh", split_axis=0, concat_axis=0, tiled=True)
        g = lax.all_gather(g, "y", axis=0, tiled=True)
        return g, lambda s: s
    if GATHER == "a2a":
        n = 32
        rep = jnp.broadcast_to(psi, (n,) + psi.shape[1:])
        g = lax.all_to_all(rep, SEC, split_axis=0, concat_axis=0, tiled=True)
        return g, lambda s: s
    raise ValueError


def reduce_out(total, slab_rows, width):
    if REDUCE == "rs":
        return lax.psum_scatter(total, OPX, scatter_dimension=0, tiled=True)
    if REDUCE == "a2a":
        parts = lax.all_to_all(total.reshape(32, slab_rows, width), OPX, split_axis=0, concat_axis=0, tiled=True)
        return jnp.sum(parts, axis=0)
    if REDUCE == "h_rs":
        t = total.reshape(8, 4, slab_rows, width).transpose(1, 0, 2, 3)
        t = lax.psum_scatter(t, "x", scatter_dimension=0, tiled=True)
        t = lax.psum_scatter(t.reshape(8, slab_rows, width), "zl", scatter_dimension=0, tiled=True)
        return t
    if REDUCE == "h_a2a_zbf":
        t = total.reshape(8, 4, slab_rows, width).transpose(1, 0, 2, 3)
        t = lax.all_to_all(t, "x", split_axis=0, concat_axis=0, tiled=True)
        t = jnp.sum(t, axis=0).astype(jnp.bfloat16)
        t = lax.all_to_all(t, "zl", split_axis=0, concat_axis=0, tiled=True)
        return jnp.sum(t.astype(jnp.float32), axis=0)
    if REDUCE == "h_a2a_xbf":
        t = total.reshape(8, 4, slab_rows, width).transpose(1, 0, 2, 3).astype(jnp.bfloat16)
        t = lax.all_to_all(t, "x", split_axis=0, concat_axis=0, tiled=True)
        t = jnp.sum(t.astype(jnp.float32), axis=0)
        t = lax.all_to_all(t, "zl", split_axis=0, concat_axis=0, tiled=True)
        return jnp.sum(t, axis=0)
    if REDUCE == "h_a2a":
        t = total.reshape(8, 4, slab_rows, width).transpose(1, 0, 2, 3)
        t = lax.all_to_all(t, "x", split_axis=0, concat_axis=0, tiled=True)
        t = jnp.sum(t, axis=0)
        t = lax.all_to_all(t, "zl", split_axis=0, concat_axis=0, tiled=True)
        return jnp.sum(t, axis=0)
    if REDUCE == "h_rs_a2a":
        t = total.reshape(8, 4, slab_rows, width).transpose(1, 0, 2, 3)
        t = lax.psum_scatter(t, "x", scatter_dimension=0, tiled=True).reshape(8, slab_rows, width)
        t = lax.all_to_all(t, "zl", split_axis=0, concat_axis=0, tiled=True)
        return jnp.sum(t, axis=0)
    if REDUCE == "h_a2a_rs":
        t = total.reshape(8, 4, slab_rows, width).transpose(1, 0, 2, 3)
        t = lax.all_to_all(t, "x", split_axis=0, concat_axis=0, tiled=True)
        t = jnp.sum(t, axis=0)
        return lax.psum_scatter(t, "zl", scatter_dimension=0, tiled=True)
    raise ValueError


def body(psi, in_sector, term_count, coef_index, left_index, term_values, left_ops, right_ops):
    ops = 32
    slab_rows = psi.shape[1]
    width = psi.shape[2]
    slabs, remap = gather_psi(psi)
    wanted = remap(in_sector[0])
    outgoing = jnp.take(slabs, wanted, axis=0, mode=TAKE)
    if ROUTE == "flat":
        arrived = lax.all_to_all(outgoing, OPX, split_axis=0, concat_axis=0, tiled=True)
    else:
        t = outgoing.reshape(8, 4, slab_rows, width).transpose(1, 0, 2, 3)
        t = lax.all_to_all(t, "x", split_axis=0, concat_axis=0, tiled=True)
        t = t.transpose(1, 0, 2, 3)
        t = lax.all_to_all(t, "zl", split_axis=0, concat_axis=0, tiled=True)
        arrived = t.reshape(32, slab_rows, width)
    block = arrived.reshape(ops * slab_rows, width)
    slots = right_ops.shape[1]
    count = term_count[0, 0]
    table_size = term_values.shape[0]
    onehot = (coef_index[0][:, None] == jnp.arange(table_size, dtype=jnp.int32)[None, :]).astype(jnp.float32)
    weights = jnp.sum(onehot * term_values[None, :], axis=1)
    live = jnp.arange(slots, dtype=jnp.int32) < count
    weights = jnp.where(live, weights, 0.0)
    if COMPUTE == "loop":
        lefts = [lax.dynamic_index_in_dim(left_ops[0], left_index[0, k], 0, keepdims=False) for k in range(slots)]
        halves = [jnp.dot(block, right_ops[0, k], preferred_element_type=jnp.float32).astype(jnp.bfloat16) for k in range(slots)]
        total = jnp.zeros((ops * slab_rows, width), jnp.float32)
        for k in range(slots):
            total = total + weights[k] * jnp.dot(lefts[k], halves[k], preferred_element_type=jnp.float32)
    else:
        lefts = jnp.take(left_ops[0], left_index[0], axis=0)
        halves = jnp.einsum("ij,kjl->kil", block, right_ops[0], preferred_element_type=jnp.float32).astype(jnp.bfloat16)
        prods = jnp.einsum("kij,kjl->kil", lefts, halves, preferred_element_type=jnp.float32)
        total = jnp.sum(weights[:, None, None] * prods, axis=0)
    mine = reduce_out(total, slab_rows, width)
    return mine.reshape(1, slab_rows, width)


def solution(mesh):
    devs = np.asarray(mesh.devices).reshape(4, 4, 2, 8, 4)
    fine = Mesh(devs, ("y", "zh", "c", "zl", "x"))
    in_specs = (
        P(SEC, OPX, None),
        P(SEC, None),
        P(SEC, OPX),
        P(SEC, OPX),
        P(SEC, OPX),
        P(),
        P(SEC, None, None, None),
        P(SEC, OPX, None, None),
    )
    out_specs = P(SEC, OPX, None)
    return jax.shard_map(body, mesh=fine, in_specs=in_specs, out_specs=out_specs, check_vma=False)
```

```python
import jax
import jax.numpy as jnp
import numpy as np
from jax import lax
from jax.sharding import Mesh, PartitionSpec as P

GATHER = "h_czy"
REDUCE = "h_a2a_xbf"
ROUTE = "flat"
COMPUTE = "batch"
TAKE = "onehot"

SEC = ("y", "zh", "c")
OPX = ("zl", "x")


def gather_psi(psi):
    if GATHER == "ag":
        g = lax.all_gather(psi, SEC, axis=0, tiled=True)
        return g, lambda s: s
    if GATHER == "h_cyz":
        g = lax.all_gather(psi, "c", axis=0, tiled=True)
        g = lax.all_gather(g, "y", axis=0, tiled=True)
        g = lax.all_gather(g, "zh", axis=0, tiled=True)
        return g, lambda s: (s % 8) // 2 * 8 + s // 8 * 2 + s % 2
    if GATHER == "h_czy":
        g = lax.all_gather(psi, "c", axis=0, tiled=True)
        g = lax.all_gather(g, "zh", axis=0, tiled=True)
        g = lax.all_gather(g, "y", axis=0, tiled=True)
        return g, lambda s: s
    if GATHER == "h_zyc":
        g = lax.all_gather(psi, "zh", axis=0, tiled=True)
        g = lax.all_gather(g, "y", axis=0, tiled=True)
        g = lax.all_gather(g, "c", axis=0, tiled=True)
        return g, lambda s: (s % 2) * 16 + (s // 8) * 4 + (s % 8) // 2
    if GATHER == "h_yzc":
        g = lax.all_gather(psi, "y", axis=0, tiled=True)
        g = lax.all_gather(g, "zh", axis=0, tiled=True)
        g = lax.all_gather(g, "c", axis=0, tiled=True)
        return g, lambda s: (s % 2) * 16 + ((s % 8) // 2) * 4 + s // 8
    if GATHER == "c_zpp_y":
        g = lax.all_gather(psi, "c", axis=0, tiled=True)
        zi = lax.axis_index("zh")
        recv = [g] + [lax.ppermute(g, "zh", [(i, (i + d) % 4) for i in range(4)]) for d in range(1, 4)]
        st = jnp.stack(recv)
        order = (zi - jnp.arange(4)) % 4
        g = jnp.take(st, order, axis=0, mode="clip").reshape((8,) + g.shape[1:])
        g = lax.all_gather(g, "y", axis=0, tiled=True)
        return g, lambda s: s
    if GATHER == "c_yz":
        g = lax.all_gather(psi, "c", axis=0, tiled=True)
        g = lax.all_gather(g, ("y", "zh"), axis=0, tiled=True)
        return g, lambda s: s
    if GATHER == "c_zpsum_y":
        g = lax.all_gather(psi, "c", axis=0, tiled=True)
        zi = lax.axis_index("zh")
        buf = jnp.zeros((4,) + g.shape, g.dtype)
        buf = lax.dynamic_update_index_in_dim(buf, g, zi, 0)
        g = lax.psum(buf, "zh").reshape((8,) + g.shape[1:])
        g = lax.all_gather(g, "y", axis=0, tiled=True)
        return g, lambda s: s
    if GATHER == "c_za2a_y":
        g = lax.all_gather(psi, "c", axis=0, tiled=True)
        rep = jnp.broadcast_to(g[None], (4,) + g.shape).reshape((8,) + g.shape[1:])
        g = lax.all_to_all(rep, "zh", split_axis=0, concat_axis=0, tiled=True)
        g = lax.all_gather(g, "y", axis=0, tiled=True)
        return g, lambda s: s
    if GATHER == "a2a":
        n = 32
        rep = jnp.broadcast_to(psi, (n,) + psi.shape[1:])
        g = lax.all_to_all(rep, SEC, split_axis=0, concat_axis=0, tiled=True)
        return g, lambda s: s
    raise ValueError


def reduce_out(total, slab_rows, width):
    if REDUCE == "rs":
        return lax.psum_scatter(total, OPX, scatter_dimension=0, tiled=True)
    if REDUCE == "a2a":
        parts = lax.all_to_all(total.reshape(32, slab_rows, width), OPX, split_axis=0, concat_axis=0, tiled=True)
        return jnp.sum(parts, axis=0)
    if REDUCE == "h_rs":
        t = total.reshape(8, 4, slab_rows, width).transpose(1, 0, 2, 3)
        t = lax.psum_scatter(t, "x", scatter_dimension=0, tiled=True)
        t = lax.psum_scatter(t.reshape(8, slab_rows, width), "zl", scatter_dimension=0, tiled=True)
        return t
    if REDUCE == "h_a2a_zbf":
        t = total.reshape(8, 4, slab_rows, width).transpose(1, 0, 2, 3)
        t = lax.all_to_all(t, "x", split_axis=0, concat_axis=0, tiled=True)
        t = jnp.sum(t, axis=0).astype(jnp.bfloat16)
        t = lax.all_to_all(t, "zl", split_axis=0, concat_axis=0, tiled=True)
        return jnp.sum(t.astype(jnp.float32), axis=0)
    if REDUCE == "h_a2a_xbf":
        t = total.reshape(8, 4, slab_rows, width).transpose(1, 0, 2, 3).astype(jnp.bfloat16)
        t = lax.all_to_all(t, "x", split_axis=0, concat_axis=0, tiled=True)
        t = jnp.sum(t.astype(jnp.float32), axis=0)
        t = lax.all_to_all(t, "zl", split_axis=0, concat_axis=0, tiled=True)
        return jnp.sum(t, axis=0)
    if REDUCE == "h_a2a":
        t = total.reshape(8, 4, slab_rows, width).transpose(1, 0, 2, 3)
        t = lax.all_to_all(t, "x", split_axis=0, concat_axis=0, tiled=True)
        t = jnp.sum(t, axis=0)
        t = lax.all_to_all(t, "zl", split_axis=0, concat_axis=0, tiled=True)
        return jnp.sum(t, axis=0)
    if REDUCE == "h_rs_a2a":
        t = total.reshape(8, 4, slab_rows, width).transpose(1, 0, 2, 3)
        t = lax.psum_scatter(t, "x", scatter_dimension=0, tiled=True).reshape(8, slab_rows, width)
        t = lax.all_to_all(t, "zl", split_axis=0, concat_axis=0, tiled=True)
        return jnp.sum(t, axis=0)
    if REDUCE == "h_a2a_rs":
        t = total.reshape(8, 4, slab_rows, width).transpose(1, 0, 2, 3)
        t = lax.all_to_all(t, "x", split_axis=0, concat_axis=0, tiled=True)
        t = jnp.sum(t, axis=0)
        return lax.psum_scatter(t, "zl", scatter_dimension=0, tiled=True)
    raise ValueError


def body(psi, in_sector, term_count, coef_index, left_index, term_values, left_ops, right_ops):
    ops = 32
    slab_rows = psi.shape[1]
    width = psi.shape[2]
    slabs, remap = gather_psi(psi)
    wanted = remap(in_sector[0])
    if TAKE == "onehot":
        pick = (wanted[:, None] == jnp.arange(slabs.shape[0], dtype=jnp.int32)[None, :]).astype(slabs.dtype)
        flat = slabs.reshape(slabs.shape[0], slab_rows * width)
        outgoing = jnp.dot(pick, flat, preferred_element_type=jnp.float32).astype(slabs.dtype).reshape(slabs.shape)
    else:
        outgoing = jnp.take(slabs, wanted, axis=0, mode=TAKE)
    if ROUTE == "flat":
        arrived = lax.all_to_all(outgoing, OPX, split_axis=0, concat_axis=0, tiled=True)
    else:
        t = outgoing.reshape(8, 4, slab_rows, width).transpose(1, 0, 2, 3)
        t = lax.all_to_all(t, "x", split_axis=0, concat_axis=0, tiled=True)
        t = t.transpose(1, 0, 2, 3)
        t = lax.all_to_all(t, "zl", split_axis=0, concat_axis=0, tiled=True)
        arrived = t.reshape(32, slab_rows, width)
    block = arrived.reshape(ops * slab_rows, width)
    slots = right_ops.shape[1]
    count = term_count[0, 0]
    table_size = term_values.shape[0]
    onehot = (coef_index[0][:, None] == jnp.arange(table_size, dtype=jnp.int32)[None, :]).astype(jnp.float32)
    weights = jnp.sum(onehot * term_values[None, :], axis=1)
    live = jnp.arange(slots, dtype=jnp.int32) < count
    weights = jnp.where(live, weights, 0.0)
    if COMPUTE == "loop":
        lefts = [lax.dynamic_index_in_dim(left_ops[0], left_index[0, k], 0, keepdims=False) for k in range(slots)]
        halves = [jnp.dot(block, right_ops[0, k], preferred_element_type=jnp.float32).astype(jnp.bfloat16) for k in range(slots)]
        total = jnp.zeros((ops * slab_rows, width), jnp.float32)
        for k in range(slots):
            total = total + weights[k] * jnp.dot(lefts[k], halves[k], preferred_element_type=jnp.float32)
    else:
        lefts = jnp.take(left_ops[0], left_index[0], axis=0)
        halves = jnp.einsum("ij,kjl->kil", block, right_ops[0], preferred_element_type=jnp.float32).astype(jnp.bfloat16)
        prods = jnp.einsum("kij,kjl->kil", lefts, halves, preferred_element_type=jnp.float32)
        total = jnp.sum(weights[:, None, None] * prods, axis=0)
    mine = reduce_out(total, slab_rows, width)
    return mine.reshape(1, slab_rows, width)


def solution(mesh):
    devs = np.asarray(mesh.devices).reshape(4, 4, 2, 8, 4)
    fine = Mesh(devs, ("y", "zh", "c", "zl", "x"))
    in_specs = (
        P(SEC, OPX, None),
        P(SEC, None),
        P(SEC, OPX),
        P(SEC, OPX),
        P(SEC, OPX),
        P(),
        P(SEC, None, None, None),
        P(SEC, OPX, None, None),
    )
    out_specs = P(SEC, OPX, None)
    return jax.shard_map(body, mesh=fine, in_specs=in_specs, out_specs=out_specs, check_vma=False)
```

```python
import jax
import jax.numpy as jnp
import numpy as np
from jax import lax
from jax.sharding import Mesh, PartitionSpec as P

GATHER = "h_czy"
REDUCE = "h_a2a"
ROUTE = "flat"
COMPUTE = "batch"
TAKE = "onehot"

SEC = ("y", "zh", "c")
OPX = ("zl", "x")


def gather_psi(psi):
    if GATHER == "ag":
        g = lax.all_gather(psi, SEC, axis=0, tiled=True)
        return g, lambda s: s
    if GATHER == "h_cyz":
        g = lax.all_gather(psi, "c", axis=0, tiled=True)
        g = lax.all_gather(g, "y", axis=0, tiled=True)
        g = lax.all_gather(g, "zh", axis=0, tiled=True)
        return g, lambda s: (s % 8) // 2 * 8 + s // 8 * 2 + s % 2
    if GATHER == "h_czy":
        g = lax.all_gather(psi, "c", axis=0, tiled=True)
        g = lax.all_gather(g, "zh", axis=0, tiled=True)
        g = lax.all_gather(g, "y", axis=0, tiled=True)
        return g, lambda s: s
    if GATHER == "h_zyc":
        g = lax.all_gather(psi, "zh", axis=0, tiled=True)
        g = lax.all_gather(g, "y", axis=0, tiled=True)
        g = lax.all_gather(g, "c", axis=0, tiled=True)
        return g, lambda s: (s % 2) * 16 + (s // 8) * 4 + (s % 8) // 2
    if GATHER == "h_yzc":
        g = lax.all_gather(psi, "y", axis=0, tiled=True)
        g = lax.all_gather(g, "zh", axis=0, tiled=True)
        g = lax.all_gather(g, "c", axis=0, tiled=True)
        return g, lambda s: (s % 2) * 16 + ((s % 8) // 2) * 4 + s // 8
    if GATHER == "c_zpp_y":
        g = lax.all_gather(psi, "c", axis=0, tiled=True)
        zi = lax.axis_index("zh")
        recv = [g] + [lax.ppermute(g, "zh", [(i, (i + d) % 4) for i in range(4)]) for d in range(1, 4)]
        st = jnp.stack(recv)
        order = (zi - jnp.arange(4)) % 4
        g = jnp.take(st, order, axis=0, mode="clip").reshape((8,) + g.shape[1:])
        g = lax.all_gather(g, "y", axis=0, tiled=True)
        return g, lambda s: s
    if GATHER == "c_yz":
        g = lax.all_gather(psi, "c", axis=0, tiled=True)
        g = lax.all_gather(g, ("y", "zh"), axis=0, tiled=True)
        return g, lambda s: s
    if GATHER == "c_zpsum_y":
        g = lax.all_gather(psi, "c", axis=0, tiled=True)
        zi = lax.axis_index("zh")
        buf = jnp.zeros((4,) + g.shape, g.dtype)
        buf = lax.dynamic_update_index_in_dim(buf, g, zi, 0)
        g = lax.psum(buf, "zh").reshape((8,) + g.shape[1:])
        g = lax.all_gather(g, "y", axis=0, tiled=True)
        return g, lambda s: s
    if GATHER == "c_za2a_y":
        g = lax.all_gather(psi, "c", axis=0, tiled=True)
        rep = jnp.broadcast_to(g[None], (4,) + g.shape).reshape((8,) + g.shape[1:])
        g = lax.all_to_all(rep, "zh", split_axis=0, concat_axis=0, tiled=True)
        g = lax.all_gather(g, "y", axis=0, tiled=True)
        return g, lambda s: s
    if GATHER == "a2a":
        n = 32
        rep = jnp.broadcast_to(psi, (n,) + psi.shape[1:])
        g = lax.all_to_all(rep, SEC, split_axis=0, concat_axis=0, tiled=True)
        return g, lambda s: s
    raise ValueError


def reduce_out(total, slab_rows, width):
    if REDUCE == "rs":
        return lax.psum_scatter(total, OPX, scatter_dimension=0, tiled=True)
    if REDUCE == "a2a":
        parts = lax.all_to_all(total.reshape(32, slab_rows, width), OPX, split_axis=0, concat_axis=0, tiled=True)
        return jnp.sum(parts, axis=0)
    if REDUCE == "h_rs":
        t = total.reshape(8, 4, slab_rows, width).transpose(1, 0, 2, 3)
        t = lax.psum_scatter(t, "x", scatter_dimension=0, tiled=True)
        t = lax.psum_scatter(t.reshape(8, slab_rows, width), "zl", scatter_dimension=0, tiled=True)
        return t
    if REDUCE == "h_a2a_zbf":
        t = total.reshape(8, 4, slab_rows, width).transpose(1, 0, 2, 3)
        t = lax.all_to_all(t, "x", split_axis=0, concat_axis=0, tiled=True)
        t = jnp.sum(t, axis=0).astype(jnp.bfloat16)
        t = lax.all_to_all(t, "zl", split_axis=0, concat_axis=0, tiled=True)
        return jnp.sum(t.astype(jnp.float32), axis=0)
    if REDUCE == "h_a2a_xbf":
        t = total.reshape(8, 4, slab_rows, width).transpose(1, 0, 2, 3).astype(jnp.bfloat16)
        t = lax.all_to_all(t, "x", split_axis=0, concat_axis=0, tiled=True)
        t = jnp.sum(t.astype(jnp.float32), axis=0)
        t = lax.all_to_all(t, "zl", split_axis=0, concat_axis=0, tiled=True)
        return jnp.sum(t, axis=0)
    if REDUCE == "h_a2a":
        t = total.reshape(8, 4, slab_rows, width).transpose(1, 0, 2, 3)
        t = lax.all_to_all(t, "x", split_axis=0, concat_axis=0, tiled=True)
        t = jnp.sum(t, axis=0)
        t = lax.all_to_all(t, "zl", split_axis=0, concat_axis=0, tiled=True)
        return jnp.sum(t, axis=0)
    if REDUCE == "h_rs_a2a":
        t = total.reshape(8, 4, slab_rows, width).transpose(1, 0, 2, 3)
        t = lax.psum_scatter(t, "x", scatter_dimension=0, tiled=True).reshape(8, slab_rows, width)
        t = lax.all_to_all(t, "zl", split_axis=0, concat_axis=0, tiled=True)
        return jnp.sum(t, axis=0)
    if REDUCE == "h_a2a_rs":
        t = total.reshape(8, 4, slab_rows, width).transpose(1, 0, 2, 3)
        t = lax.all_to_all(t, "x", split_axis=0, concat_axis=0, tiled=True)
        t = jnp.sum(t, axis=0)
        return lax.psum_scatter(t, "zl", scatter_dimension=0, tiled=True)
    raise ValueError


def body(psi, in_sector, term_count, coef_index, left_index, term_values, left_ops, right_ops):
    ops = 32
    slab_rows = psi.shape[1]
    width = psi.shape[2]
    slabs, remap = gather_psi(psi)
    wanted = remap(in_sector[0])
    if TAKE == "onehot":
        pick = (wanted[:, None] == jnp.arange(slabs.shape[0], dtype=jnp.int32)[None, :]).astype(slabs.dtype)
        flat = slabs.reshape(slabs.shape[0], slab_rows * width)
        outgoing = jnp.dot(pick, flat, preferred_element_type=jnp.float32).astype(slabs.dtype).reshape(slabs.shape)
    else:
        outgoing = jnp.take(slabs, wanted, axis=0, mode=TAKE)
    if ROUTE == "flat":
        arrived = lax.all_to_all(outgoing, OPX, split_axis=0, concat_axis=0, tiled=True)
    else:
        t = outgoing.reshape(8, 4, slab_rows, width).transpose(1, 0, 2, 3)
        t = lax.all_to_all(t, "x", split_axis=0, concat_axis=0, tiled=True)
        t = t.transpose(1, 0, 2, 3)
        t = lax.all_to_all(t, "zl", split_axis=0, concat_axis=0, tiled=True)
        arrived = t.reshape(32, slab_rows, width)
    block = arrived.reshape(ops * slab_rows, width)
    slots = right_ops.shape[1]
    count = term_count[0, 0]
    table_size = term_values.shape[0]
    onehot = (coef_index[0][:, None] == jnp.arange(table_size, dtype=jnp.int32)[None, :]).astype(jnp.float32)
    weights = jnp.sum(onehot * term_values[None, :], axis=1)
    live = jnp.arange(slots, dtype=jnp.int32) < count
    weights = jnp.where(live, weights, 0.0)
    if COMPUTE == "loop":
        lefts = [lax.dynamic_index_in_dim(left_ops[0], left_index[0, k], 0, keepdims=False) for k in range(slots)]
        halves = [jnp.dot(block, right_ops[0, k], preferred_element_type=jnp.float32).astype(jnp.bfloat16) for k in range(slots)]
        total = jnp.zeros((ops * slab_rows, width), jnp.float32)
        for k in range(slots):
            total = total + weights[k] * jnp.dot(lefts[k], halves[k], preferred_element_type=jnp.float32)
    else:
        lefts = jnp.take(left_ops[0], left_index[0], axis=0)
        halves = jnp.einsum("ij,kjl->kil", block, right_ops[0], preferred_element_type=jnp.float32).astype(jnp.bfloat16)
        prods = jnp.einsum("kij,kjl->kil", lefts, halves, preferred_element_type=jnp.float32)
        total = jnp.sum(weights[:, None, None] * prods, axis=0)
    mine = reduce_out(total, slab_rows, width)
    return mine.reshape(1, slab_rows, width)


def solution(mesh):
    devs = np.asarray(mesh.devices).reshape(4, 4, 2, 8, 4)
    fine = Mesh(devs, ("y", "zh", "c", "zl", "x"))
    in_specs = (
        P(SEC, OPX, None),
        P(SEC, None),
        P(SEC, OPX),
        P(SEC, OPX),
        P(SEC, OPX),
        P(),
        P(SEC, None, None, None),
        P(SEC, OPX, None, None),
    )
    out_specs = P(SEC, OPX, None)
    return jax.shard_map(body, mesh=fine, in_specs=in_specs, out_specs=out_specs, check_vma=False)
```

```python
import jax
import jax.numpy as jnp
import numpy as np
from jax import lax
from jax.sharding import Mesh, PartitionSpec as P

GATHER = "h_czy"
REDUCE = "h_a2a_xbf"
ROUTE = "flat"
COMPUTE = "batch"
TAKE = "onehot"

SEC = ("y", "zh", "c")
OPX = ("zl", "x")


def gather_psi(psi):
    if GATHER == "ag":
        g = lax.all_gather(psi, SEC, axis=0, tiled=True)
        return g, lambda s: s
    if GATHER == "h_cyz":
        g = lax.all_gather(psi, "c", axis=0, tiled=True)
        g = lax.all_gather(g, "y", axis=0, tiled=True)
        g = lax.all_gather(g, "zh", axis=0, tiled=True)
        return g, lambda s: (s % 8) // 2 * 8 + s // 8 * 2 + s % 2
    if GATHER == "h_czy":
        g = lax.all_gather(psi, "c", axis=0, tiled=True)
        g = lax.all_gather(g, "zh", axis=0, tiled=True)
        g = lax.all_gather(g, "y", axis=0, tiled=True)
        return g, lambda s: s
    if GATHER == "h_zyc":
        g = lax.all_gather(psi, "zh", axis=0, tiled=True)
        g = lax.all_gather(g, "y", axis=0, tiled=True)
        g = lax.all_gather(g, "c", axis=0, tiled=True)
        return g, lambda s: (s % 2) * 16 + (s // 8) * 4 + (s % 8) // 2
    if GATHER == "h_yzc":
        g = lax.all_gather(psi, "y", axis=0, tiled=True)
        g = lax.all_gather(g, "zh", axis=0, tiled=True)
        g = lax.all_gather(g, "c", axis=0, tiled=True)
        return g, lambda s: (s % 2) * 16 + ((s % 8) // 2) * 4 + s // 8
    if GATHER == "c_zpp_y":
        g = lax.all_gather(psi, "c", axis=0, tiled=True)
        zi = lax.axis_index("zh")
        recv = [g] + [lax.ppermute(g, "zh", [(i, (i + d) % 4) for i in range(4)]) for d in range(1, 4)]
        st = jnp.stack(recv)
        order = (zi - jnp.arange(4)) % 4
        g = jnp.take(st, order, axis=0, mode="clip").reshape((8,) + g.shape[1:])
        g = lax.all_gather(g, "y", axis=0, tiled=True)
        return g, lambda s: s
    if GATHER == "c_yz":
        g = lax.all_gather(psi, "c", axis=0, tiled=True)
        g = lax.all_gather(g, ("y", "zh"), axis=0, tiled=True)
        return g, lambda s: s
    if GATHER == "c_zpsum_y":
        g = lax.all_gather(psi, "c", axis=0, tiled=True)
        zi = lax.axis_index("zh")
        buf = jnp.zeros((4,) + g.shape, g.dtype)
        buf = lax.dynamic_update_index_in_dim(buf, g, zi, 0)
        g = lax.psum(buf, "zh").reshape((8,) + g.shape[1:])
        g = lax.all_gather(g, "y", axis=0, tiled=True)
        return g, lambda s: s
    if GATHER == "c_za2a_y":
        g = lax.all_gather(psi, "c", axis=0, tiled=True)
        rep = jnp.broadcast_to(g[None], (4,) + g.shape).reshape((8,) + g.shape[1:])
        g = lax.all_to_all(rep, "zh", split_axis=0, concat_axis=0, tiled=True)
        g = lax.all_gather(g, "y", axis=0, tiled=True)
        return g, lambda s: s
    if GATHER == "a2a":
        n = 32
        rep = jnp.broadcast_to(psi, (n,) + psi.shape[1:])
        g = lax.all_to_all(rep, SEC, split_axis=0, concat_axis=0, tiled=True)
        return g, lambda s: s
    raise ValueError


def reduce_out(total, slab_rows, width):
    if REDUCE == "rs":
        return lax.psum_scatter(total, OPX, scatter_dimension=0, tiled=True)
    if REDUCE == "a2a":
        parts = lax.all_to_all(total.reshape(32, slab_rows, width), OPX, split_axis=0, concat_axis=0, tiled=True)
        return jnp.sum(parts, axis=0)
    if REDUCE == "h_rs":
        t = total.reshape(8, 4, slab_rows, width).transpose(1, 0, 2, 3)
        t = lax.psum_scatter(t, "x", scatter_dimension=0, tiled=True)
        t = lax.psum_scatter(t.reshape(8, slab_rows, width), "zl", scatter_dimension=0, tiled=True)
        return t
    if REDUCE == "h_a2a_zbf":
        t = total.reshape(8, 4, slab_rows, width).transpose(1, 0, 2, 3)
        t = lax.all_to_all(t, "x", split_axis=0, concat_axis=0, tiled=True)
        t = jnp.sum(t, axis=0).astype(jnp.bfloat16)
        t = lax.all_to_all(t, "zl", split_axis=0, concat_axis=0, tiled=True)
        return jnp.sum(t.astype(jnp.float32), axis=0)
    if REDUCE == "h_a2a_xbf":
        t = total.reshape(8, 4, slab_rows, width).transpose(1, 0, 2, 3).astype(jnp.bfloat16)
        t = lax.all_to_all(t, "x", split_axis=0, concat_axis=0, tiled=True)
        t = jnp.sum(t.astype(jnp.float32), axis=0)
        t = lax.all_to_all(t, "zl", split_axis=0, concat_axis=0, tiled=True)
        return jnp.sum(t, axis=0)
    if REDUCE == "h_a2a":
        t = total.reshape(8, 4, slab_rows, width).transpose(1, 0, 2, 3)
        t = lax.all_to_all(t, "x", split_axis=0, concat_axis=0, tiled=True)
        t = jnp.sum(t, axis=0)
        t = lax.all_to_all(t, "zl", split_axis=0, concat_axis=0, tiled=True)
        return jnp.sum(t, axis=0)
    if REDUCE == "h_rs_a2a":
        t = total.reshape(8, 4, slab_rows, width).transpose(1, 0, 2, 3)
        t = lax.psum_scatter(t, "x", scatter_dimension=0, tiled=True).reshape(8, slab_rows, width)
        t = lax.all_to_all(t, "zl", split_axis=0, concat_axis=0, tiled=True)
        return jnp.sum(t, axis=0)
    if REDUCE == "h_a2a_rs":
        t = total.reshape(8, 4, slab_rows, width).transpose(1, 0, 2, 3)
        t = lax.all_to_all(t, "x", split_axis=0, concat_axis=0, tiled=True)
        t = jnp.sum(t, axis=0)
        return lax.psum_scatter(t, "zl", scatter_dimension=0, tiled=True)
    raise ValueError


def body(psi, in_sector, term_count, coef_index, left_index, term_values, left_ops, right_ops):
    ops = 32
    slab_rows = psi.shape[1]
    width = psi.shape[2]
    slabs, remap = gather_psi(psi)
    wanted = remap(in_sector[0])
    if TAKE == "onehot":
        pick = (wanted[:, None] == jnp.arange(slabs.shape[0], dtype=jnp.int32)[None, :]).astype(slabs.dtype)
        outgoing = jnp.einsum("od,dij->oij", pick, slabs, preferred_element_type=jnp.float32).astype(slabs.dtype)
    else:
        outgoing = jnp.take(slabs, wanted, axis=0, mode=TAKE)
    if ROUTE == "flat":
        arrived = lax.all_to_all(outgoing, OPX, split_axis=0, concat_axis=0, tiled=True)
    else:
        t = outgoing.reshape(8, 4, slab_rows, width).transpose(1, 0, 2, 3)
        t = lax.all_to_all(t, "x", split_axis=0, concat_axis=0, tiled=True)
        t = t.transpose(1, 0, 2, 3)
        t = lax.all_to_all(t, "zl", split_axis=0, concat_axis=0, tiled=True)
        arrived = t.reshape(32, slab_rows, width)
    block = arrived.reshape(ops * slab_rows, width)
    slots = right_ops.shape[1]
    count = term_count[0, 0]
    table_size = term_values.shape[0]
    onehot = (coef_index[0][:, None] == jnp.arange(table_size, dtype=jnp.int32)[None, :]).astype(jnp.float32)
    weights = jnp.sum(onehot * term_values[None, :], axis=1)
    live = jnp.arange(slots, dtype=jnp.int32) < count
    weights = jnp.where(live, weights, 0.0)
    if COMPUTE == "loop":
        lefts = [lax.dynamic_index_in_dim(left_ops[0], left_index[0, k], 0, keepdims=False) for k in range(slots)]
        halves = [jnp.dot(block, right_ops[0, k], preferred_element_type=jnp.float32).astype(jnp.bfloat16) for k in range(slots)]
        total = jnp.zeros((ops * slab_rows, width), jnp.float32)
        for k in range(slots):
            total = total + weights[k] * jnp.dot(lefts[k], halves[k], preferred_element_type=jnp.float32)
    else:
        lefts = jnp.take(left_ops[0], left_index[0], axis=0)
        halves = jnp.einsum("ij,kjl->kil", block, right_ops[0], preferred_element_type=jnp.float32).astype(jnp.bfloat16)
        prods = jnp.einsum("kij,kjl->kil", lefts, halves, preferred_element_type=jnp.float32)
        total = jnp.sum(weights[:, None, None] * prods, axis=0)
    mine = reduce_out(total, slab_rows, width)
    return mine.reshape(1, slab_rows, width)


def solution(mesh):
    devs = np.asarray(mesh.devices).reshape(4, 4, 2, 8, 4)
    fine = Mesh(devs, ("y", "zh", "c", "zl", "x"))
    in_specs = (
        P(SEC, OPX, None),
        P(SEC, None),
        P(SEC, OPX),
        P(SEC, OPX),
        P(SEC, OPX),
        P(),
        P(SEC, None, None, None),
        P(SEC, OPX, None, None),
    )
    out_specs = P(SEC, OPX, None)
    return jax.shard_map(body, mesh=fine, in_specs=in_specs, out_specs=out_specs, check_vma=False)
```

```python
import jax
import jax.numpy as jnp
import numpy as np
from jax import lax
from jax.sharding import Mesh, PartitionSpec as P

GATHER = "h_czy"
REDUCE = "h_a2a_xbf"
ROUTE = "flat"
COMPUTE = "batch"
TAKE = "onehot"

SEC = ("y", "zh", "c")
OPX = ("zl", "x")


def gather_psi(psi):
    if GATHER == "ag":
        g = lax.all_gather(psi, SEC, axis=0, tiled=True)
        return g, lambda s: s
    if GATHER == "h_cyz":
        g = lax.all_gather(psi, "c", axis=0, tiled=True)
        g = lax.all_gather(g, "y", axis=0, tiled=True)
        g = lax.all_gather(g, "zh", axis=0, tiled=True)
        return g, lambda s: (s % 8) // 2 * 8 + s // 8 * 2 + s % 2
    if GATHER == "h_czy":
        g = lax.all_gather(psi, "c", axis=0, tiled=True)
        g = lax.all_gather(g, "zh", axis=0, tiled=True)
        g = lax.all_gather(g, "y", axis=0, tiled=True)
        return g, lambda s: s
    if GATHER == "h_zyc":
        g = lax.all_gather(psi, "zh", axis=0, tiled=True)
        g = lax.all_gather(g, "y", axis=0, tiled=True)
        g = lax.all_gather(g, "c", axis=0, tiled=True)
        return g, lambda s: (s % 2) * 16 + (s // 8) * 4 + (s % 8) // 2
    if GATHER == "h_yzc":
        g = lax.all_gather(psi, "y", axis=0, tiled=True)
        g = lax.all_gather(g, "zh", axis=0, tiled=True)
        g = lax.all_gather(g, "c", axis=0, tiled=True)
        return g, lambda s: (s % 2) * 16 + ((s % 8) // 2) * 4 + s // 8
    if GATHER == "c_zpp_y":
        g = lax.all_gather(psi, "c", axis=0, tiled=True)
        zi = lax.axis_index("zh")
        recv = [g] + [lax.ppermute(g, "zh", [(i, (i + d) % 4) for i in range(4)]) for d in range(1, 4)]
        st = jnp.stack(recv)
        order = (zi - jnp.arange(4)) % 4
        g = jnp.take(st, order, axis=0, mode="clip").reshape((8,) + g.shape[1:])
        g = lax.all_gather(g, "y", axis=0, tiled=True)
        return g, lambda s: s
    if GATHER == "c_yz":
        g = lax.all_gather(psi, "c", axis=0, tiled=True)
        g = lax.all_gather(g, ("y", "zh"), axis=0, tiled=True)
        return g, lambda s: s
    if GATHER == "c_zpsum_y":
        g = lax.all_gather(psi, "c", axis=0, tiled=True)
        zi = lax.axis_index("zh")
        buf = jnp.zeros((4,) + g.shape, g.dtype)
        buf = lax.dynamic_update_index_in_dim(buf, g, zi, 0)
        g = lax.psum(buf, "zh").reshape((8,) + g.shape[1:])
        g = lax.all_gather(g, "y", axis=0, tiled=True)
        return g, lambda s: s
    if GATHER == "c_za2a_y":
        g = lax.all_gather(psi, "c", axis=0, tiled=True)
        rep = jnp.broadcast_to(g[None], (4,) + g.shape).reshape((8,) + g.shape[1:])
        g = lax.all_to_all(rep, "zh", split_axis=0, concat_axis=0, tiled=True)
        g = lax.all_gather(g, "y", axis=0, tiled=True)
        return g, lambda s: s
    if GATHER == "a2a":
        n = 32
        rep = jnp.broadcast_to(psi, (n,) + psi.shape[1:])
        g = lax.all_to_all(rep, SEC, split_axis=0, concat_axis=0, tiled=True)
        return g, lambda s: s
    raise ValueError


def reduce_out(total, slab_rows, width):
    if REDUCE == "rs":
        return lax.psum_scatter(total, OPX, scatter_dimension=0, tiled=True)
    if REDUCE == "a2a":
        parts = lax.all_to_all(total.reshape(32, slab_rows, width), OPX, split_axis=0, concat_axis=0, tiled=True)
        return jnp.sum(parts, axis=0)
    if REDUCE == "h_rs":
        t = total.reshape(8, 4, slab_rows, width).transpose(1, 0, 2, 3)
        t = lax.psum_scatter(t, "x", scatter_dimension=0, tiled=True)
        t = lax.psum_scatter(t.reshape(8, slab_rows, width), "zl", scatter_dimension=0, tiled=True)
        return t
    if REDUCE == "h_a2a_zbf":
        t = total.reshape(8, 4, slab_rows, width).transpose(1, 0, 2, 3)
        t = lax.all_to_all(t, "x", split_axis=0, concat_axis=0, tiled=True)
        t = jnp.sum(t, axis=0).astype(jnp.bfloat16)
        t = lax.all_to_all(t, "zl", split_axis=0, concat_axis=0, tiled=True)
        return jnp.sum(t.astype(jnp.float32), axis=0)
    if REDUCE == "h_a2a_xbf":
        t = total.reshape(4, 8, slab_rows, width).astype(jnp.bfloat16)
        t = lax.all_to_all(t, "x", split_axis=0, concat_axis=0, tiled=True)
        t = jnp.sum(t.astype(jnp.float32), axis=0)
        t = lax.all_to_all(t, "zl", split_axis=0, concat_axis=0, tiled=True)
        return jnp.sum(t, axis=0)
    if REDUCE == "h_a2a":
        t = total.reshape(8, 4, slab_rows, width).transpose(1, 0, 2, 3)
        t = lax.all_to_all(t, "x", split_axis=0, concat_axis=0, tiled=True)
        t = jnp.sum(t, axis=0)
        t = lax.all_to_all(t, "zl", split_axis=0, concat_axis=0, tiled=True)
        return jnp.sum(t, axis=0)
    if REDUCE == "h_rs_a2a":
        t = total.reshape(8, 4, slab_rows, width).transpose(1, 0, 2, 3)
        t = lax.psum_scatter(t, "x", scatter_dimension=0, tiled=True).reshape(8, slab_rows, width)
        t = lax.all_to_all(t, "zl", split_axis=0, concat_axis=0, tiled=True)
        return jnp.sum(t, axis=0)
    if REDUCE == "h_a2a_rs":
        t = total.reshape(8, 4, slab_rows, width).transpose(1, 0, 2, 3)
        t = lax.all_to_all(t, "x", split_axis=0, concat_axis=0, tiled=True)
        t = jnp.sum(t, axis=0)
        return lax.psum_scatter(t, "zl", scatter_dimension=0, tiled=True)
    raise ValueError


def body(psi, in_sector, term_count, coef_index, left_index, term_values, left_ops, right_ops):
    ops = 32
    slab_rows = psi.shape[1]
    width = psi.shape[2]
    slabs, remap = gather_psi(psi)
    wanted = remap(in_sector[0])
    if TAKE == "onehot":
        pick = (wanted[:, None] == jnp.arange(slabs.shape[0], dtype=jnp.int32)[None, :]).astype(slabs.dtype)
        outgoing = jnp.einsum("od,dij->oij", pick, slabs, preferred_element_type=jnp.float32).astype(slabs.dtype)
    else:
        outgoing = jnp.take(slabs, wanted, axis=0, mode=TAKE)
    if ROUTE == "flat":
        arrived = lax.all_to_all(outgoing, OPX, split_axis=0, concat_axis=0, tiled=True)
    else:
        t = outgoing.reshape(8, 4, slab_rows, width).transpose(1, 0, 2, 3)
        t = lax.all_to_all(t, "x", split_axis=0, concat_axis=0, tiled=True)
        t = t.transpose(1, 0, 2, 3)
        t = lax.all_to_all(t, "zl", split_axis=0, concat_axis=0, tiled=True)
        arrived = t.reshape(32, slab_rows, width)
    block = arrived.reshape(ops * slab_rows, width)
    slots = right_ops.shape[1]
    count = term_count[0, 0]
    table_size = term_values.shape[0]
    onehot = (coef_index[0][:, None] == jnp.arange(table_size, dtype=jnp.int32)[None, :]).astype(jnp.float32)
    weights = jnp.sum(onehot * term_values[None, :], axis=1)
    live = jnp.arange(slots, dtype=jnp.int32) < count
    weights = jnp.where(live, weights, 0.0)
    if COMPUTE == "loop":
        lefts = [lax.dynamic_index_in_dim(left_ops[0], left_index[0, k], 0, keepdims=False) for k in range(slots)]
        halves = [jnp.dot(block, right_ops[0, k], preferred_element_type=jnp.float32).astype(jnp.bfloat16) for k in range(slots)]
        total = jnp.zeros((ops * slab_rows, width), jnp.float32)
        for k in range(slots):
            total = total + weights[k] * jnp.dot(lefts[k], halves[k], preferred_element_type=jnp.float32)
    else:
        lefts = jnp.take(left_ops[0], left_index[0], axis=0)
        lefts = lefts.reshape(slots, 8, 4, slab_rows, width).transpose(0, 2, 1, 3, 4).reshape(slots, 32 * slab_rows, width)
        halves = jnp.einsum("ij,kjl->kil", block, right_ops[0], preferred_element_type=jnp.float32).astype(jnp.bfloat16)
        prods = jnp.einsum("kij,kjl->kil", lefts, halves, preferred_element_type=jnp.float32)
        total = jnp.sum(weights[:, None, None] * prods, axis=0)
    mine = reduce_out(total, slab_rows, width)
    return mine.reshape(1, slab_rows, width)


def solution(mesh):
    devs = np.asarray(mesh.devices).reshape(4, 4, 2, 8, 4)
    fine = Mesh(devs, ("y", "zh", "c", "zl", "x"))
    in_specs = (
        P(SEC, OPX, None),
        P(SEC, None),
        P(SEC, OPX),
        P(SEC, OPX),
        P(SEC, OPX),
        P(),
        P(SEC, None, None, None),
        P(SEC, OPX, None, None),
    )
    out_specs = P(SEC, OPX, None)
    return jax.shard_map(body, mesh=fine, in_specs=in_specs, out_specs=out_specs, check_vma=False)
```
